512 devices in a mesh: section: 8 (over y, core), dp: 64 (over x, z).
Axes of the slice: x: 4, y: 4, z: 16, core: 2. Of those that a mesh axis runs over, the one named last changes fastest.
Arguments:
- queries: bfloat16 [8, 8192, 2560], P('section', 'dp')
- key_cells: bfloat16 [8, 8192, 2560], P('section', 'dp')
- value_cells: bfloat16 [8, 8192, 2560], P('section', 'dp'), may hold values from -6 to 6
- grad_cells: bfloat16 [8, 8192, 2560], P('section', 'dp'), may hold values from -6 to 6
- packing: int32 [8, 64, 128], P('section', 'dp'), may hold values from 0 to 127, each once within a row
- segment_ids: int32 [8, 8192], P('section'), may hold values from 0 to 511, never falling along the last dimension, each value on 1 to 32 neighbouring positions
Outputs:
- input_grads: bfloat16 [8, 8192, 7680], P('section', 'dp')
The draws below stay inside these ranges and needn't reach their ends.
Inputs may be any that keep to these rules, and one draw needn't show every extreme that they name: `packing`: each row of a section and device is a permutation of 0 to 127. `segment_ids`: along a section's packed cells the ids never fall; each segment has 1 to 32 cells and one has exactly 32.
All inputs are finite; a program needn't handle non-finite values.
Results may differ from the reference program's by a relative error of at most 0.0086.
Values may be sent and summed in bfloat16 or wider, within the bound.
No kernel may reach another device: no remote copies, remote signals or barrier semaphores. Data moves between devices by JAX's collectives and lax.ppermute only.
A program may use at most 64 MiB of HBM per device.

```python
import math
import jax
import jax.numpy as jnp
import numpy as np
from jax import lax

HEADS = 20
HEAD_DIM = 128
ROWS = 128
FEAT = 2560
SECTIONS = 8
TOKENS = 8192
PER_PEER = 2
REACH = 32
SEGS = 512
N_DP = 64


def draw_queries(key, part):
    noise = jax.random.normal(jax.random.fold_in(key, 1), (SECTIONS, TOKENS, FEAT), jnp.float32)
    values = jnp.clip(noise, -6.0, 6.0)
    return values.astype(jnp.bfloat16)


def draw_key_cells(key, part):
    noise = jax.random.normal(jax.random.fold_in(key, 2), (SECTIONS, TOKENS, FEAT), jnp.float32)
    values = jnp.clip(noise, -6.0, 6.0)
    return values.astype(jnp.bfloat16)


def level_of(stream_key, shape, cuts, low, high):
    loudness, own = 1.0, jax.random.fold_in(stream_key, 6)
    for dim, parts in cuts:
        draws = jnp.exp(jax.random.uniform(jax.random.fold_in(own, dim), (parts,), jnp.float32, low / len(cuts), high / len(cuts)))
        loudness = loudness * jnp.repeat(draws, shape[dim] // parts).reshape([-1 if axis == dim else 1 for axis in range(len(shape))])
    return loudness


def length_profile(amount, total, reach, slope):
    weights = [(1 << 20) // math.isqrt(grade ** slope) + 1 for grade in range(2, amount + 1)]
    surplus, given = total - reach - (amount - 1), [1] * (amount - 1)
    while surplus > 0:
        free = [i for i in range(amount - 1) if given[i] < reach]
        whole, remaining = sum([weights[i] for i in free]), surplus
        for i in free:
            extra = min(reach - given[i], max(1, remaining * weights[i] // whole), surplus)
            given[i] = given[i] + extra
            surplus = surplus - extra
    return np.array([reach] + given)


def uneven_parts(own_key, amount, total, limit, skew):
    if amount == 2:
        one = jax.random.randint(own_key, (), max(1, total - limit), min(limit, total - 1) + 1)
        return jnp.stack([one, total - one])
    lengths = jnp.asarray(length_profile(amount, total, limit, skew), jnp.int32)
    twos = (amount - 1) // 2
    giver, sink = lengths[1:1 + 2 * twos:2], lengths[2:2 + 2 * twos:2]
    slack = jnp.minimum(giver - 1, limit - sink)
    passed = jax.random.randint(jax.random.fold_in(own_key, 1), (twos,), 0, 1 << 20) % (slack + 1)
    lengths = lengths.at[1:1 + 2 * twos:2].set(giver - passed).at[2:2 + 2 * twos:2].set(sink + passed)
    return lengths[jax.random.permutation(jax.random.fold_in(own_key, 2), amount)]


def bell_draw(own_key, extent, scale, limit, cuts=(), kind=jnp.bfloat16):
    entries = jax.random.normal(own_key, extent, jnp.float32) * scale
    if len(cuts) > 0:
        entries = level_of(own_key, extent, cuts, -0.22, 0.18) * entries
    return jnp.clip(entries, min=-limit, max=limit).astype(kind)


def setup_inputs(seed: int = 0) -> dict:
    arg_keys = jax.random.split(jax.random.key(seed), 7)
    queries = draw_queries(jax.random.fold_in(arg_keys[6], 71), 0)
    key_cells = draw_key_cells(jax.random.fold_in(arg_keys[6], 71), 0)
    value_cells = bell_draw(arg_keys[2], (SECTIONS, TOKENS, FEAT), 1.0, 6.0, ((0, 8), (1, 64)))
    grad_cells = bell_draw(arg_keys[3], (SECTIONS, TOKENS, FEAT), 1.0, 6.0, ((0, 8), (1, 64)))
    packing = jax.vmap(lambda own: jax.random.permutation(own, ROWS))(jax.random.split(arg_keys[4], SECTIONS * N_DP)).reshape((SECTIONS, N_DP, ROWS)).astype(jnp.int32)
    segment_ids = jax.vmap(lambda own: jnp.searchsorted(jnp.cumsum(uneven_parts(own, SEGS, TOKENS, REACH, 2)), jnp.arange(TOKENS), side="right"))(jax.random.split(arg_keys[5], SECTIONS)).reshape((SECTIONS, TOKENS)).astype(jnp.int32)
    return dict(queries=queries, key_cells=key_cells, value_cells=value_cells, grad_cells=grad_cells, packing=packing, segment_ids=segment_ids)


def split_heads(matrix):
    return matrix.astype(jnp.float32).reshape(matrix.shape[0], HEADS, HEAD_DIM)


def block_grads(query_block, key_window, value_window, grad_block, query_ids, key_ids):
    scale = HEAD_DIM ** -0.5
    query_heads = split_heads(query_block)
    key_heads = split_heads(key_window)
    value_heads = split_heads(value_window)
    grad_heads = split_heads(grad_block)
    scores = jnp.einsum('ihd,jhd->hij', query_heads, key_heads) * scale
    allowed = (query_ids[:, None] == key_ids[None, :])[None]
    scores = jnp.where(allowed, scores, -jnp.inf)
    top = jnp.max(scores, axis=2)
    log_total = top + jnp.log(jnp.sum(jnp.exp(scores - top[:, :, None]), axis=2))
    probs = jnp.exp(scores - log_total[:, :, None])
    probs_low = lax.optimization_barrier(probs.astype(jnp.bfloat16)).astype(jnp.float32)
    attended = jnp.einsum('hij,jhd->ihd', probs_low, value_heads)
    delta = jnp.sum(grad_heads * attended, axis=2).T
    dprobs = jnp.einsum('ihd,jhd->hij', grad_heads, value_heads)
    dscores = (probs * (dprobs - delta[:, :, None]) * scale).astype(jnp.bfloat16)
    dscores = lax.optimization_barrier(dscores).astype(jnp.float32)
    grad_query = jnp.einsum('hij,jhd->ihd', dscores, key_heads).reshape(query_block.shape[0], FEAT)
    grad_key = jnp.einsum('hij,ihd->jhd', dscores, query_heads).reshape(key_window.shape[0], FEAT)
    grad_value = jnp.einsum('hij,ihd->jhd', probs_low, grad_heads).reshape(key_window.shape[0], FEAT)
    return grad_query.astype(jnp.bfloat16), jnp.concatenate([grad_key, grad_value], axis=1)


def section_grads(queries, key_cells, value_cells, grad_cells, packing, segment_ids):
    cells = jnp.arange(TOKENS, dtype=jnp.int32)
    block_of = cells // ROWS
    source = (cells % ROWS) // PER_PEER
    slot = cells % PER_PEER
    anchor = (source * ROWS + packing[source, block_of * PER_PEER + slot]).astype(jnp.int32)
    packed_q = queries[anchor]
    packed_g = grad_cells[anchor]
    edge = jnp.zeros((REACH, FEAT), jnp.bfloat16)
    padded_k = jnp.concatenate([edge, key_cells[anchor], edge], axis=0)
    padded_v = jnp.concatenate([edge, value_cells[anchor], edge], axis=0)
    rim_ids = jnp.full((REACH,), -1, jnp.int32)
    padded_ids = jnp.concatenate([rim_ids, segment_ids.astype(jnp.int32), rim_ids])
    window = ROWS + 2 * REACH

    def step(totals, block):
        start = (block * ROWS).astype(jnp.int32)
        query_block = lax.dynamic_slice_in_dim(packed_q, start, ROWS)
        grad_block = lax.dynamic_slice_in_dim(packed_g, start, ROWS)
        key_window = lax.dynamic_slice_in_dim(padded_k, start, window)
        value_window = lax.dynamic_slice_in_dim(padded_v, start, window)
        key_ids = lax.dynamic_slice_in_dim(padded_ids, start, window)
        query_ids = lax.dynamic_slice_in_dim(padded_ids, start + REACH, ROWS)
        grad_query, partial_value = block_grads(query_block, key_window, value_window, grad_block, query_ids, key_ids)
        before = lax.dynamic_slice_in_dim(totals, start, window)
        totals = lax.dynamic_update_slice_in_dim(totals, before + partial_value, start, 0)
        return totals, grad_query

    start_totals = jnp.zeros((TOKENS + 2 * REACH, 2 * FEAT), jnp.float32)
    totals, query_grads = lax.scan(step, start_totals, jnp.arange(N_DP, dtype=jnp.int32))
    key_value = totals[REACH:REACH + TOKENS].astype(jnp.bfloat16)
    packed_grads = jnp.concatenate([query_grads.reshape(TOKENS, FEAT), key_value], axis=1)
    return jnp.zeros_like(packed_grads).at[anchor].set(packed_grads)


def reference(queries, key_cells, value_cells, grad_cells, packing, segment_ids):
    grads = lax.map(lambda items: section_grads(*items), (queries, key_cells, value_cells, grad_cells, packing, segment_ids))
    return jnp.roll(grads, -1, axis=0)
```

```python
import jax
import jax.numpy as jnp
from jax import lax
from jax.sharding import PartitionSpec as P

HEADS = 20
HEAD_DIM = 128
CHUNKS = 1


def with_halo(value, axis, width):
    size, length = (lax.axis_size(axis), value.shape[0])
    up = [(i, (i + 1) % size) for i in range(size - 1)]
    down = [(j, i) for i, j in up]
    before = lax.ppermute(value[length - width :], axis, up)
    after = lax.ppermute(value[:width], axis, down)
    return jnp.concatenate([before, value, after], axis=0)


def passed_along(value, axis, steps):
    count = lax.axis_size(axis)
    initial, last = (max(0, -steps), min(count, count - steps))
    return lax.ppermute(value, axis, [(source, source + steps) for source in range(initial, last)])


def from_behind(block, axis, distance):
    devices = range(lax.axis_size(axis))
    route = [((i - distance) % len(devices), i) for i in devices]
    return lax.ppermute(block, axis, route)


def heads_of(matrix):
    return matrix.reshape(matrix.shape[0], -1, HEAD_DIM)


def chunk_grads(own_q, own_k, own_v, own_g, own_ids, window_ids, reach):
    cell_count, width = own_q.shape
    scale = HEAD_DIM ** (-0.5)
    key_value = jnp.concatenate([own_k, own_v], axis=1)
    key_value_window = with_halo(key_value, "dp", reach)
    key_window = key_value_window[:, :width]
    value_window = key_value_window[:, width:]
    scores = jnp.einsum(
        "ihd,jhd->hij", heads_of(own_q), heads_of(key_window), preferred_element_type=jnp.float32
    )
    scores = scores * scale
    allowed = (own_ids[:, None] == window_ids[None, :])[None]
    scores = jnp.where(allowed, scores, -jnp.inf)
    top = jnp.max(scores, axis=2)
    log_total = top + jnp.log(jnp.sum(jnp.exp(scores - top[:, :, None]), axis=2))
    probs = jnp.exp(scores - log_total[:, :, None])
    probs_low = probs.astype(jnp.bfloat16)
    grad_heads = heads_of(own_g)
    attended = jnp.einsum(
        "hij,jhd->ihd", probs_low, heads_of(value_window), preferred_element_type=jnp.float32
    )
    delta = jnp.sum(grad_heads.astype(jnp.float32) * attended, axis=2).T
    dprobs = jnp.einsum(
        "ihd,jhd->hij", grad_heads, heads_of(value_window), preferred_element_type=jnp.float32
    )
    dscores = (probs * (dprobs - delta[:, :, None]) * scale).astype(jnp.bfloat16)
    grad_query = jnp.einsum(
        "hij,jhd->ihd", dscores, heads_of(key_window), preferred_element_type=jnp.float32
    )
    grad_query = grad_query.reshape(cell_count, width).astype(jnp.bfloat16)
    window = cell_count + 2 * reach
    grad_key = jnp.einsum(
        "hij,ihd->jhd", dscores, heads_of(own_q), preferred_element_type=jnp.float32
    )
    grad_value = jnp.einsum(
        "hij,ihd->jhd", probs_low, grad_heads, preferred_element_type=jnp.float32
    )
    partial_value = jnp.concatenate(
        [grad_key.reshape(window, width), grad_value.reshape(window, width)], axis=1
    )
    from_after = passed_along(partial_value[:reach].astype(jnp.bfloat16), "dp", -1).astype(
        jnp.float32
    )
    from_before = passed_along(
        partial_value[reach + cell_count :].astype(jnp.bfloat16), "dp", 1
    ).astype(jnp.float32)
    summed = partial_value[reach : reach + cell_count]
    summed = summed.at[cell_count - reach :].add(from_after)
    summed = summed.at[:reach].add(from_before)
    return jnp.concatenate([grad_query, summed.astype(jnp.bfloat16)], axis=1)


def body(queries, key_cells, value_cells, grad_cells, packing, segment_ids):
    cell_count = queries.shape[1]
    width = queries.shape[2]
    groups = lax.axis_size("dp")
    per_peer = cell_count // groups
    reach = cell_count // 4
    place = lax.axis_index("dp")
    order = packing[0, 0]
    part = width // CHUNKS

    rim_ids = jnp.full((reach,), -1, jnp.int32)
    padded_ids = jnp.concatenate([rim_ids, segment_ids[0], rim_ids])
    window_ids = lax.dynamic_slice_in_dim(padded_ids, place * cell_count, cell_count + 2 * reach)
    own_ids = window_ids[reach : reach + cell_count]
    inverse = (
        jnp.zeros((cell_count,), jnp.int32).at[order].set(jnp.arange(cell_count, dtype=jnp.int32))
    )
    sources = (queries[0], key_cells[0], value_cells[0], grad_cells[0])
    pieces = []
    for c in range(CHUNKS):
        cols = slice(c * part, (c + 1) * part)
        stacked = jnp.concatenate([m[:, cols] for m in sources], axis=1)[order]
        arrived = lax.all_to_all(
            stacked.reshape(groups, per_peer, 4 * part), "dp", split_axis=0, concat_axis=0, tiled=True
        ).reshape(cell_count, 4 * part)
        own_q, own_k, own_v, own_g = [arrived[:, i * part : (i + 1) * part] for i in range(4)]
        packed_grads = chunk_grads(own_q, own_k, own_v, own_g, own_ids, window_ids, reach)
        returned = lax.all_to_all(
            packed_grads.reshape(groups, per_peer, 3 * part),
            "dp",
            split_axis=0,
            concat_axis=0,
            tiled=True,
        ).reshape(cell_count, 3 * part)
        pieces.append(from_behind(returned[inverse], "section", -1))
    ordered = [piece[:, i * part : (i + 1) * part] for i in range(3) for piece in pieces]
    return jnp.concatenate(ordered, axis=1)[None]


def solution(mesh):
    return jax.shard_map(
        body,
        mesh=mesh,
        in_specs=(
            P("section", "dp", None),
            P("section", "dp", None),
            P("section", "dp", None),
            P("section", "dp", None),
            P("section", "dp", None),
            P("section", None),
        ),
        out_specs=P("section", "dp", None),
        check_vma=False,
    )
```

```python
import jax
import jax.numpy as jnp
from jax import lax
from jax.sharding import PartitionSpec as P

HEADS = 20
HEAD_DIM = 128


def with_halo(value, axis, width):
    size, length = (lax.axis_size(axis), value.shape[0])
    up = [(i, (i + 1) % size) for i in range(size - 1)]
    down = [(j, i) for i, j in up]
    before = lax.ppermute(value[length - width :], axis, up)
    after = lax.ppermute(value[:width], axis, down)
    return jnp.concatenate([before, value, after], axis=0)


def passed_along(value, axis, steps):
    count = lax.axis_size(axis)
    initial, last = (max(0, -steps), min(count, count - steps))
    return lax.ppermute(value, axis, [(source, source + steps) for source in range(initial, last)])


def from_behind(block, axis, distance):
    devices = range(lax.axis_size(axis))
    route = [((i - distance) % len(devices), i) for i in devices]
    return lax.ppermute(block, axis, route)


def heads_of(matrix):
    return matrix.reshape(matrix.shape[0], -1, HEAD_DIM)


def chunk_grads(own_q, own_k, own_v, own_g, own_ids, window_ids, reach):
    cell_count, width = own_q.shape
    scale = HEAD_DIM ** (-0.5)
    key_value = jnp.concatenate([own_k, own_v], axis=1)
    key_value_window = with_halo(key_value, "dp", reach)
    key_window = key_value_window[:, :width]
    value_window = key_value_window[:, width:]
    scores = jnp.einsum(
        "ihd,jhd->hij", heads_of(own_q), heads_of(key_window), preferred_element_type=jnp.float32
    )
    scores = scores * scale
    allowed = (own_ids[:, None] == window_ids[None, :])[None]
    scores = jnp.where(allowed, scores, -jnp.inf)
    top = jnp.max(scores, axis=2)
    log_total = top + jnp.log(jnp.sum(jnp.exp(scores - top[:, :, None]), axis=2))
    probs = jnp.exp(scores - log_total[:, :, None])
    probs_low = probs.astype(jnp.bfloat16)
    grad_heads = heads_of(own_g)
    attended = jnp.einsum(
        "hij,jhd->ihd", probs_low, heads_of(value_window), preferred_element_type=jnp.float32
    )
    delta = jnp.sum(grad_heads.astype(jnp.float32) * attended, axis=2).T
    dprobs = jnp.einsum(
        "ihd,jhd->hij", grad_heads, heads_of(value_window), preferred_element_type=jnp.float32
    )
    dscores = (probs * (dprobs - delta[:, :, None]) * scale).astype(jnp.bfloat16)
    grad_query = jnp.einsum(
        "hij,jhd->ihd", dscores, heads_of(key_window), preferred_element_type=jnp.float32
    )
    grad_query = grad_query.reshape(cell_count, width).astype(jnp.bfloat16)
    window = cell_count + 2 * reach
    grad_key = jnp.einsum(
        "hij,ihd->jhd", dscores, heads_of(own_q), preferred_element_type=jnp.float32
    )
    grad_value = jnp.einsum(
        "hij,ihd->jhd", probs_low, grad_heads, preferred_element_type=jnp.float32
    )
    partial_value = jnp.concatenate(
        [grad_key.reshape(window, width), grad_value.reshape(window, width)], axis=1
    )
    from_after = passed_along(partial_value[:reach].astype(jnp.bfloat16), "dp", -1).astype(
        jnp.float32
    )
    from_before = passed_along(
        partial_value[reach + cell_count :].astype(jnp.bfloat16), "dp", 1
    ).astype(jnp.float32)
    summed = partial_value[reach : reach + cell_count]
    summed = summed.at[cell_count - reach :].add(from_after)
    summed = summed.at[:reach].add(from_before)
    return grad_query, summed.astype(jnp.bfloat16)


def body(queries, key_cells, value_cells, grad_cells, packing, segment_ids):
    cell_count = queries.shape[1]
    width = queries.shape[2]
    groups = lax.axis_size("dp")
    per_peer = cell_count // groups
    reach = cell_count // 4
    place = lax.axis_index("dp")
    order = packing[0, 0]

    rim_ids = jnp.full((reach,), -1, jnp.int32)
    padded_ids = jnp.concatenate([rim_ids, segment_ids[0], rim_ids])
    window_ids = lax.dynamic_slice_in_dim(padded_ids, place * cell_count, cell_count + 2 * reach)
    own_ids = window_ids[reach : reach + cell_count]
    sources = (queries[0], key_cells[0], value_cells[0], grad_cells[0])
    next_order = from_behind(order, "section", -1)
    cells = jnp.arange(cell_count, dtype=jnp.int32)
    picking = (order.reshape(groups, per_peer)[:, :, None] == cells).astype(jnp.bfloat16)
    placing = (next_order.reshape(groups, per_peer)[None] == cells[:, None, None]).astype(jnp.bfloat16)
    stacked = jnp.einsum(
        "bgr,rf->bgf", picking, jnp.concatenate(sources, axis=1), preferred_element_type=jnp.float32
    ).astype(jnp.bfloat16)
    arrived = lax.all_to_all(stacked, "dp", split_axis=0, concat_axis=0, tiled=True)
    arrived = arrived.reshape(cell_count, 4 * width)
    own_q, own_k, own_v, own_g = [arrived[:, i * width : (i + 1) * width] for i in range(4)]
    grad_query, summed = chunk_grads(own_q, own_k, own_v, own_g, own_ids, window_ids, reach)
    next_query = from_behind(grad_query, "section", -1)
    returned = lax.all_to_all(
        jnp.concatenate([next_query, summed], axis=1).reshape(groups, per_peer, 3 * width),
        "dp",
        split_axis=0,
        concat_axis=0,
        tiled=True,
    )
    handed = from_behind(returned[:, :, width:], "section", -1)
    arranged = jnp.concatenate([returned[:, :, :width], handed], axis=2)
    loaded = jnp.einsum("kbg,bgf->kf", placing, arranged, preferred_element_type=jnp.float32)
    return loaded.astype(jnp.bfloat16)[None]


def solution(mesh):
    return jax.shard_map(
        body,
        mesh=mesh,
        in_specs=(
            P("section", "dp", None),
            P("section", "dp", None),
            P("section", "dp", None),
            P("section", "dp", None),
            P("section", "dp", None),
            P("section", None),
        ),
        out_specs=P("section", "dp", None),
        check_vma=False,
    )
```

```python
import jax
import jax.numpy as jnp
from jax import lax
from jax.sharding import PartitionSpec as P

HEADS = 20
HEAD_DIM = 128


def with_halo(value, edges, axis):
    size = lax.axis_size(axis)
    up = [(i, i + 1) for i in range(size - 1)]
    down = [(j, i) for i, j in up]
    head, tail = edges
    before = lax.ppermute(tail, axis, up)
    after = lax.ppermute(head, axis, down)
    return jnp.concatenate([before, value, after], axis=0)


def passed_along(value, axis, steps):
    count = lax.axis_size(axis)
    initial, last = (max(0, -steps), min(count, count - steps))
    return lax.ppermute(value, axis, [(source, source + steps) for source in range(initial, last)])


def from_behind(block, axis, distance):
    devices = range(lax.axis_size(axis))
    route = [((i - distance) % len(devices), i) for i in devices]
    return lax.ppermute(block, axis, route)


def heads_of(matrix):
    return matrix.reshape(matrix.shape[0], -1, HEAD_DIM)


def chunk_grads(own_q, own_k, own_v, own_g, edges, own_ids, window_ids, reach):
    cell_count, width = own_q.shape
    scale = HEAD_DIM ** (-0.5)
    key_value = jnp.concatenate([own_k, own_v], axis=1)
    key_value_window = with_halo(key_value, edges, "dp")
    key_window = key_value_window[:, :width]
    value_window = key_value_window[:, width:]
    scores = jnp.einsum(
        "ihd,jhd->hij", heads_of(own_q), heads_of(key_window), preferred_element_type=jnp.float32
    )
    scores = scores * scale
    allowed = (own_ids[:, None] == window_ids[None, :])[None]
    scores = jnp.where(allowed, scores, -jnp.inf)
    top = jnp.max(scores, axis=2)
    log_total = top + jnp.log(jnp.sum(jnp.exp(scores - top[:, :, None]), axis=2))
    probs = jnp.exp(scores - log_total[:, :, None])
    probs_low = probs.astype(jnp.bfloat16)
    grad_heads = heads_of(own_g)
    attended = jnp.einsum(
        "hij,jhd->ihd", probs_low, heads_of(value_window), preferred_element_type=jnp.float32
    )
    delta = jnp.sum(grad_heads.astype(jnp.float32) * attended, axis=2).T
    dprobs = jnp.einsum(
        "ihd,jhd->hij", grad_heads, heads_of(value_window), preferred_element_type=jnp.float32
    )
    dscores = (probs * (dprobs - delta[:, :, None]) * scale).astype(jnp.bfloat16)
    grad_query = jnp.einsum(
        "hij,jhd->ihd", dscores, heads_of(key_window), preferred_element_type=jnp.float32
    )
    grad_query = grad_query.reshape(cell_count, width).astype(jnp.bfloat16)
    window = cell_count + 2 * reach
    grad_key = jnp.einsum(
        "hij,ihd->jhd", dscores, heads_of(own_q), preferred_element_type=jnp.float32
    )
    grad_value = jnp.einsum(
        "hij,ihd->jhd", probs_low, grad_heads, preferred_element_type=jnp.float32
    )
    partial_value = jnp.concatenate(
        [grad_key.reshape(window, width), grad_value.reshape(window, width)], axis=1
    )
    from_after = passed_along(partial_value[:reach].astype(jnp.bfloat16), "dp", -1).astype(
        jnp.float32
    )
    from_before = passed_along(
        partial_value[reach + cell_count :].astype(jnp.bfloat16), "dp", 1
    ).astype(jnp.float32)
    summed = partial_value[reach : reach + cell_count]
    summed = summed.at[cell_count - reach :].add(from_after)
    summed = summed.at[:reach].add(from_before)
    return grad_query, summed.astype(jnp.bfloat16)


def body(queries, key_cells, value_cells, grad_cells, packing, segment_ids):
    cell_count = queries.shape[1]
    width = queries.shape[2]
    groups = lax.axis_size("dp")
    per_peer = cell_count // groups
    reach = cell_count // 4
    place = lax.axis_index("dp")
    order = packing[0, 0]

    rim_ids = jnp.full((reach,), -1, jnp.int32)
    padded_ids = jnp.concatenate([rim_ids, segment_ids[0], rim_ids])
    window_ids = lax.dynamic_slice_in_dim(padded_ids, place * cell_count, cell_count + 2 * reach)
    own_ids = window_ids[reach : reach + cell_count]
    sources = (queries[0], key_cells[0], value_cells[0], grad_cells[0])
    next_order = from_behind(order, "section", -1)
    cells = jnp.arange(cell_count, dtype=jnp.int32)
    picking = (order.reshape(groups, per_peer)[:, :, None] == cells).astype(jnp.bfloat16)
    placing = (next_order.reshape(groups, per_peer)[None] == cells[:, None, None]).astype(jnp.bfloat16)
    stacked = jnp.einsum(
        "bgr,rf->bgf", picking, jnp.concatenate(sources, axis=1), preferred_element_type=jnp.float32
    ).astype(jnp.bfloat16)
    arrived = lax.all_to_all(stacked, "dp", split_axis=0, concat_axis=0, tiled=True)
    edge_blocks = reach // per_peer
    edges = (
        arrived[:edge_blocks, :, width : 3 * width].reshape(reach, 2 * width),
        arrived[groups - edge_blocks :, :, width : 3 * width].reshape(reach, 2 * width),
    )
    arrived = arrived.reshape(cell_count, 4 * width)
    own_q, own_k, own_v, own_g = [arrived[:, i * width : (i + 1) * width] for i in range(4)]
    grad_query, summed = chunk_grads(
        own_q, own_k, own_v, own_g, edges, own_ids, window_ids, reach
    )
    next_query = from_behind(grad_query, "section", -1)
    returned = lax.all_to_all(
        jnp.concatenate([next_query, summed], axis=1).reshape(groups, per_peer, 3 * width),
        "dp",
        split_axis=0,
        concat_axis=0,
        tiled=True,
    )
    handed = from_behind(returned[:, :, width:], "section", -1)
    arranged = jnp.concatenate([returned[:, :, :width], handed], axis=2)
    loaded = jnp.einsum("kbg,bgf->kf", placing, arranged, preferred_element_type=jnp.float32)
    return loaded.astype(jnp.bfloat16)[None]


def solution(mesh):
    return jax.shard_map(
        body,
        mesh=mesh,
        in_specs=(
            P("section", "dp", None),
            P("section", "dp", None),
            P("section", "dp", None),
            P("section", "dp", None),
            P("section", "dp", None),
            P("section", None),
        ),
        out_specs=P("section", "dp", None),
        check_vma=False,
    )
```

```python
import jax
import jax.numpy as jnp
from jax import lax
from jax.sharding import PartitionSpec as P

HEADS = 20
HEAD_DIM = 128


def with_halo(value, edges, axis):
    size = lax.axis_size(axis)
    up = [(i, i + 1) for i in range(size - 1)]
    down = [(j, i) for i, j in up]
    head, tail = edges
    before = lax.ppermute(tail, axis, up).reshape(-1, value.shape[1])
    after = lax.ppermute(head, axis, down).reshape(-1, value.shape[1])
    return jnp.concatenate([before, value, after], axis=0)


def passed_along(value, axis, steps):
    count = lax.axis_size(axis)
    initial, last = (max(0, -steps), min(count, count - steps))
    return lax.ppermute(value, axis, [(source, source + steps) for source in range(initial, last)])


def from_behind(block, axis, distance):
    devices = range(lax.axis_size(axis))
    route = [((i - distance) % len(devices), i) for i in devices]
    return lax.ppermute(block, axis, route)


def heads_of(matrix):
    return matrix.reshape(matrix.shape[0], -1, HEAD_DIM)


def chunk_grads(own_q, own_k, own_v, own_g, edges, own_ids, window_ids, reach):
    cell_count, width = own_q.shape
    scale = HEAD_DIM ** (-0.5)
    key_value = jnp.concatenate([own_k, own_v], axis=1)
    key_value_window = with_halo(key_value, edges, "dp")
    key_window = key_value_window[:, :width]
    value_window = key_value_window[:, width:]
    scores = jnp.einsum(
        "ihd,jhd->hij", heads_of(own_q), heads_of(key_window), preferred_element_type=jnp.float32
    )
    scores = scores * scale
    allowed = (own_ids[:, None] == window_ids[None, :])[None]
    scores = jnp.where(allowed, scores, -jnp.inf)
    top = jnp.max(scores, axis=2)
    log_total = top + jnp.log(jnp.sum(jnp.exp(scores - top[:, :, None]), axis=2))
    probs = jnp.exp(scores - log_total[:, :, None])
    probs_low = probs.astype(jnp.bfloat16)
    grad_heads = heads_of(own_g)
    attended = jnp.einsum(
        "hij,jhd->ihd", probs_low, heads_of(value_window), preferred_element_type=jnp.float32
    )
    delta = jnp.sum(grad_heads.astype(jnp.float32) * attended, axis=2).T
    dprobs = jnp.einsum(
        "ihd,jhd->hij", grad_heads, heads_of(value_window), preferred_element_type=jnp.float32
    )
    dscores = (probs * (dprobs - delta[:, :, None]) * scale).astype(jnp.bfloat16)
    grad_query = jnp.einsum(
        "hij,jhd->ihd", dscores, heads_of(key_window), preferred_element_type=jnp.float32
    )
    grad_query = grad_query.reshape(cell_count, width).astype(jnp.bfloat16)
    window = cell_count + 2 * reach
    grad_key = jnp.einsum(
        "hij,ihd->jhd", dscores, heads_of(own_q), preferred_element_type=jnp.float32
    )
    grad_value = jnp.einsum(
        "hij,ihd->jhd", probs_low, grad_heads, preferred_element_type=jnp.float32
    )
    partial_value = jnp.concatenate(
        [grad_key.reshape(window, width), grad_value.reshape(window, width)], axis=1
    )
    from_after = passed_along(partial_value[:reach].astype(jnp.bfloat16), "dp", -1).astype(
        jnp.float32
    )
    from_before = passed_along(
        partial_value[reach + cell_count :].astype(jnp.bfloat16), "dp", 1
    ).astype(jnp.float32)
    summed = partial_value[reach : reach + cell_count]
    summed = summed.at[cell_count - reach :].add(from_after)
    summed = summed.at[:reach].add(from_before)
    return grad_query, summed.astype(jnp.bfloat16)


def body(queries, key_cells, value_cells, grad_cells, packing, segment_ids):
    cell_count = queries.shape[1]
    width = queries.shape[2]
    groups = lax.axis_size("dp")
    per_peer = cell_count // groups
    reach = cell_count // 4
    place = lax.axis_index("dp")
    order = packing[0, 0]

    rim_ids = jnp.full((reach,), -1, jnp.int32)
    padded_ids = jnp.concatenate([rim_ids, segment_ids[0], rim_ids])
    window_ids = lax.dynamic_slice_in_dim(padded_ids, place * cell_count, cell_count + 2 * reach)
    own_ids = window_ids[reach : reach + cell_count]
    sources = (queries[0], key_cells[0], value_cells[0], grad_cells[0])
    next_order = from_behind(order, "section", -1)
    cells = jnp.arange(cell_count, dtype=jnp.int32)
    picking = (order.reshape(groups, per_peer)[:, :, None] == cells).astype(jnp.bfloat16)
    placing = (next_order.reshape(groups, per_peer)[None] == cells[:, None, None]).astype(jnp.bfloat16)
    stacked = jnp.einsum(
        "bgr,rf->bgf", picking, jnp.concatenate(sources, axis=1), preferred_element_type=jnp.float32
    ).astype(jnp.bfloat16)
    arrived = lax.all_to_all(stacked, "dp", split_axis=0, concat_axis=0, tiled=True)
    edge_blocks = reach // per_peer
    edges = (
        arrived[:edge_blocks, :, width : 3 * width],
        arrived[groups - edge_blocks :, :, width : 3 * width],
    )
    arrived = arrived.reshape(cell_count, 4 * width)
    own_q, own_k, own_v, own_g = [arrived[:, i * width : (i + 1) * width] for i in range(4)]
    grad_query, summed = chunk_grads(
        own_q, own_k, own_v, own_g, edges, own_ids, window_ids, reach
    )
    next_query = from_behind(grad_query, "section", -1)
    returned = lax.all_to_all(
        jnp.concatenate([next_query, summed], axis=1).reshape(groups, per_peer, 3 * width),
        "dp",
        split_axis=0,
        concat_axis=0,
        tiled=True,
    )
    handed = from_behind(returned[:, :, width:], "section", -1)
    arranged = jnp.concatenate([returned[:, :, :width], handed], axis=2)
    loaded = jnp.einsum("kbg,bgf->kf", placing, arranged, preferred_element_type=jnp.float32)
    return loaded.astype(jnp.bfloat16)[None]


def solution(mesh):
    return jax.shard_map(
        body,
        mesh=mesh,
        in_specs=(
            P("section", "dp", None),
            P("section", "dp", None),
            P("section", "dp", None),
            P("section", "dp", None),
            P("section", "dp", None),
            P("section", None),
        ),
        out_specs=P("section", "dp", None),
        check_vma=False,
    )
```
